512 devices in a mesh: dp: 16 (over y, core), cell: 32 (over x, z).
Axes of the slice: x: 4, y: 8, z: 8, core: 2. Of those that a mesh axis runs over, the one named last changes fastest.
Arguments:
- sensitivity: bfloat16 [2048, 200704], P('dp', 'cell'), may hold values from -0.0390625 to 0.0390625
- direction: bfloat16 [16, 200704], P(None, 'cell'), may hold values from -6 to 6
- depth_weight: float32 [200704], P('cell'), may hold values from 0.3 to 3
- counts: int32 [32], P('cell'), may hold values from 4704 to 6272, as said below
- send_lists: int32 [32, 2, 128], P('cell'), may hold values from 0 to 6271, as said below
- neighbours: int32 [6, 200704], P(None, 'cell'), may hold values from 0 to 6528, as said below
Outputs:
- product: float32 [16, 200704], P(None, 'cell')
The draws below stay inside these ranges and needn't reach their ends.
Inputs may be any that keep to these rules, and one draw needn't show every extreme that they name: `counts`: every partition has at least 4704 live cells; some partition is full in every draw. `send_lists`: entries are local indices of live cells of their own partition. `neighbours`: entries below 6272 are live local cells that differ from the cell's own local index by at most 64; 6272 to 6527 name received rim cells; 6528 is an absent face; padded slots hold only absent faces.
All inputs are finite; a program needn't handle non-finite values.
Results may differ from the reference program's by a relative error of at most 0.0008.
Values sent between devices are 32-bit elements; how exact they have to be, the bound alone decides.
No kernel may reach another device: no remote copies, remote signals or barrier semaphores. Data moves between devices by JAX's collectives and lax.ppermute only.
A program may use at most 64 MiB of HBM per device.

```python
import math
import jax
import jax.numpy as jnp
from jax import lax

C_DEV = 6272
NV = 16
RIM = 128
K = 6
NDATA = 2048
NPART = 32
NCELLS = 200704


def part_counts(key):
    base = jax.random.fold_in(key, 11)
    drawn = jax.random.randint(base, (NPART,), 3 * C_DEV // 4, C_DEV + 1)
    full = jax.random.randint(jax.random.fold_in(base, 1), (), 0, NPART)
    return (jnp.where(jnp.arange(NPART) == full, C_DEV, drawn).astype(jnp.int32), full)


def draw_counts(key, part):
    sizes, full = part_counts(key)
    return sizes


def draw_send_lists(key, part):
    sizes, full = part_counts(key)
    raw = jax.random.randint(jax.random.fold_in(key, 22), (NPART, 2, RIM), 0, 1 << 20)
    lists = (raw % sizes[:, None, None]).astype(jnp.int32)
    rows = jnp.arange(NPART, dtype=jnp.int32)[:, None, None]
    sides = jnp.arange(2, dtype=jnp.int32)[None, :, None]
    spots = jnp.arange(RIM, dtype=jnp.int32)[None, None, :]
    first = (rows == full) & (spots == 0)
    lists = jnp.where(first & (sides == 0), C_DEV - 1, lists)
    lists = jnp.where(first & (sides == 1), 0, lists)
    return lists.astype(jnp.int32)


def draw_neighbours(key, part):
    sizes, full = part_counts(key)
    base = jax.random.fold_in(key, 33)
    kinds = jax.random.randint(jax.random.fold_in(base, 1), (K, NPART, C_DEV), 0, 8)
    offset = jax.random.randint(jax.random.fold_in(base, 2), (K, NPART, C_DEV), -64, 65)
    rimpick = jax.random.randint(jax.random.fold_in(base, 3), (K, NPART, C_DEV), 0, 2 * RIM)
    position = jnp.arange(C_DEV, dtype=jnp.int32)[None, None, :]
    limit = sizes[None, :, None]
    nearby = jnp.clip(position + offset, 0, limit - 1)
    sentinel = C_DEV + 2 * RIM
    chosen = jnp.where(kinds < 5, nearby, jnp.where(kinds == 5, C_DEV + rimpick, sentinel))
    chosen = jnp.where(position < limit, chosen, sentinel)
    return chosen.reshape(K, NPART * C_DEV).astype(jnp.int32)


def shard_levels(rng, dims, shards, least, high):
    factor_of = 1.0
    for dim, shards_of in shards:
        steps = jax.random.uniform(jax.random.fold_in(jax.random.fold_in(rng, 6), dim), (shards_of,), jnp.float32, least / len(shards), high / len(shards))
        factor_of = factor_of * jnp.repeat(jnp.exp(steps), dims[dim] // shards_of).reshape((-1,) + (1,) * (len(dims) - 1 - dim))
    return factor_of


def normal_values(key, shape, scale, most, shards=(), held_as=jnp.bfloat16):
    level = shard_levels(key, shape, shards, -0.22, 0.18) if shards else 1.0
    values = jax.random.normal(key, shape, jnp.float32) * scale * level
    return jnp.minimum(jnp.maximum(values, -most), most).astype(held_as)


def setup_inputs(seed: int = 0) -> dict:
    streams_of = jax.random.split(jax.random.key(seed), 7)
    sensitivity = normal_values(streams_of[0], (NDATA, NCELLS), ((NCELLS * NDATA) ** 0.5) ** -0.5, 0.0390625, ((0, 16), (1, 32)))
    direction = normal_values(streams_of[1], (NV, NCELLS), 1.0, 6.0, ((1, 32),))
    depth_weight = jnp.clip(jnp.exp(math.log(3.0) - 2.3025851 * jax.random.uniform(streams_of[2], (NCELLS,), jnp.float32) ** shard_levels(streams_of[2], (NCELLS,), ((0, 32),), -0.2, 0.2)), 0.3, 3.0)
    counts = draw_counts(jax.random.fold_in(streams_of[6], 71), 0)
    send_lists = draw_send_lists(jax.random.fold_in(streams_of[6], 71), 0)
    neighbours = draw_neighbours(jax.random.fold_in(streams_of[6], 71), 0)
    return {"sensitivity": sensitivity, "direction": direction, "depth_weight": depth_weight, "counts": counts, "send_lists": send_lists, "neighbours": neighbours}


def reference(sensitivity, direction, depth_weight, counts, send_lists, neighbours):
    slots = jnp.arange(NCELLS, dtype=jnp.int32)
    local = slots % C_DEV
    owner = slots // C_DEV
    live = local < counts[owner]
    masked = jnp.where(live[None, :], direction, jnp.zeros_like(direction)).astype(jnp.bfloat16)
    predicted = lax.dot_general(masked, sensitivity, (((1,), (1,)), ((), ())), preferred_element_type=jnp.float32)
    rounded = predicted.astype(jnp.bfloat16)
    remainder = (predicted - rounded.astype(jnp.float32)).astype(jnp.bfloat16)
    stacked = jnp.concatenate([rounded, remainder], axis=0)
    both = jnp.dot(stacked, sensitivity, preferred_element_type=jnp.float32)
    misfit = both[:NV] + both[NV:]
    weight = jnp.where(live, depth_weight, jnp.float32(0.0))
    values = jnp.concatenate([masked.astype(jnp.float32), weight[None, :]], axis=0)
    blocks = values.reshape(NV + 1, NPART, C_DEV)
    index = jnp.broadcast_to(send_lists.reshape(1, NPART, 2 * RIM), (NV + 1, NPART, 2 * RIM))
    sent = jnp.take_along_axis(blocks, index, axis=2)
    lower = sent[:, :, :RIM]
    upper = sent[:, :, RIM:]
    zero_rim = jnp.zeros((NV + 1, 1, RIM), jnp.float32)
    prev_upper = jnp.concatenate([zero_rim, upper[:, :-1]], axis=1)
    next_lower = jnp.concatenate([lower[:, 1:], zero_rim], axis=1)
    extended = jnp.concatenate([blocks, prev_upper, next_lower, jnp.zeros((NV + 1, NPART, 1), jnp.float32)], axis=2)
    width = extended.shape[2]
    faces = neighbours.reshape(K, NPART, C_DEV)
    big_ext = jnp.broadcast_to(extended[:, None], (NV + 1, K, NPART, width))
    big_idx = jnp.broadcast_to(faces[None], (NV + 1, K, NPART, C_DEV))
    found = jnp.take_along_axis(big_ext, big_idx, axis=3)
    own_p = blocks[:NV]
    own_w = blocks[NV]
    near_w = found[NV]
    near_p = found[:NV]
    coupling = jnp.sum(near_w[None] * (own_p[:, None] - near_p), axis=1)
    smooth = own_w[None] * own_w[None] * own_p + own_w[None] * coupling
    total = misfit + 0.5 * smooth.reshape(NV, NCELLS)
    return jnp.where(live[None, :], total, jnp.float32(0.0))
```

```python
import jax
import jax.numpy as jnp
from jax import lax
from jax.sharding import PartitionSpec as P


def padded_2(value, sides, width):
    for axis, dim in sides:
        count, length = (lax.axis_size(axis), value.shape[dim])
        up = [(i, (i + 1) % count) for i in range(count - 1)]
        down = [(j, i) for i, j in up]
        last = lax.slice_in_dim(value, length - width, length, axis=dim)
        leading = lax.slice_in_dim(value, 0, width, axis=dim)
        before = lax.ppermute(last, axis, up)
        after = lax.ppermute(leading, axis, down)
        value = jnp.concatenate([before, value, after], axis=dim)
    return value


def butterfly_sum(value, axis):
    count = lax.axis_size(axis)
    step = 1
    while step < count:
        pairs = [(j, j ^ step) for j in range(count)]
        value = value + lax.ppermute(value, axis, pairs)
        step *= 2
    return value


def halving_sum(value, axis):
    count = lax.axis_size(axis)
    me = lax.axis_index(axis)
    steps = []
    step = 1
    while step < count:
        steps.append(step)
        step *= 2
    for step in steps:
        half = value.shape[0] // 2
        low, high = value[:half], value[half:]
        upper = (me & step) != 0
        keep = jnp.where(upper, high, low)
        send = jnp.where(upper, low, high)
        pairs = [(j, j ^ step) for j in range(count)]
        value = keep + lax.ppermute(send, axis, pairs)
    for step in reversed(steps):
        pairs = [(j, j ^ step) for j in range(count)]
        other = lax.ppermute(value, axis, pairs)
        upper = (me & step) != 0
        low = jnp.where(upper, other, value)
        high = jnp.where(upper, value, other)
        value = jnp.concatenate([low, high], axis=0)
    return value


def pick_block():
    block_len = 8
    for candidate in range(128, 7, -8):
        block_len = candidate
        break
    return block_len


def pick_group(block_count):
    group_len = 1
    for candidate in range(1, 9):
        if block_count % candidate == 0:
            group_len = candidate
    return group_len


def smoothness(masked_f, weight, send_lists, neighbours, width):
    slots = masked_f.shape[1]
    values = jnp.concatenate([masked_f * weight[None, :], weight[None, :]], axis=0)
    picked = jnp.take(values, send_lists[0].reshape(-1), axis=1)
    rim = picked.shape[1] // 2
    padded = padded_2(picked, (("cell", 1),), rim)
    rim_vals = jnp.concatenate([padded[:, :rim], padded[:, 3 * rim :]], axis=1)
    lanes = values.shape[0]
    block_len = pick_block()
    block_count = width // block_len
    pieces = 1 + (128 + block_len - 1) // block_len
    spread = jnp.pad(values, ((0, 0), (64, pieces * block_len)))
    local_vals = lax.slice_in_dim(spread, 0, (block_count + pieces - 1) * block_len, axis=1)
    shifted = [
        local_vals[:, m * block_len : (m + block_count) * block_len].reshape(
            lanes, block_count, block_len
        )
        for m in range(pieces)
    ]
    rim_part = jnp.broadcast_to(rim_vals[:, None, :], (lanes, block_count, 2 * rim))
    windows = jnp.concatenate(shifted + [rim_part], axis=2).transpose(1, 0, 2)
    span = windows.shape[2]
    position = jnp.arange(width, dtype=jnp.int32)
    anchor = position // block_len * block_len
    column = jnp.where(
        neighbours < slots,
        neighbours - anchor[None, :] + 64,
        jnp.where(neighbours < slots + 2 * rim, pieces * block_len + neighbours - slots, -1),
    )
    column = column.reshape(neighbours.shape[0], block_count, block_len).transpose(1, 0, 2)
    group_len = pick_group(block_count)
    windows = windows.reshape(block_count // group_len, group_len, lanes, span)
    column = column.reshape(block_count // group_len, group_len, neighbours.shape[0], block_len)

    def gather_block(item):
        window_set, column_set = item
        target = jnp.arange(span, dtype=jnp.int32)[None, None, :, None]
        hits = jnp.sum((column_set[:, :, None, :] == target).astype(jnp.float32), axis=1)
        return jnp.einsum("grw,gwb->grb", window_set, hits, precision=lax.Precision.HIGHEST)

    sums = lax.map(gather_block, (windows, column))
    sums = sums.reshape(block_count, lanes, block_len).transpose(1, 0, 2).reshape(lanes, width)
    coupling = masked_f * sums[-1][None, :] - sums[:-1]
    return weight[None] * weight[None] * masked_f + weight[None] * coupling


def on_device(sensitivity, direction, depth_weight, counts, send_lists, neighbours):
    slots = sensitivity.shape[1]
    nvecs = direction.shape[0]
    live = jnp.arange(slots, dtype=jnp.int32) < counts[0]
    masked = jnp.where(live[None, :], direction, jnp.zeros_like(direction))
    partial_data = lax.dot_general(
        masked, sensitivity, (((1,), (1,)), ((), ())), preferred_element_type=jnp.float32
    )
    summed = butterfly_sum(partial_data, "cell")
    rounded = summed.astype(jnp.bfloat16)
    remainder = (summed - rounded.astype(jnp.float32)).astype(jnp.bfloat16)
    stacked = jnp.concatenate([rounded, remainder], axis=0)
    both = jnp.dot(stacked, sensitivity, preferred_element_type=jnp.float32)
    partial_cells = both[:nvecs] + both[nvecs:]
    weight = jnp.where(live, depth_weight, jnp.float32(0.0))
    masked_f = masked.astype(jnp.float32)
    misfit = halving_sum(partial_cells, "dp")
    smooth = smoothness(masked_f, weight, send_lists, neighbours, slots)
    total = misfit + 0.5 * smooth
    return jnp.where(live[None, :], total, jnp.float32(0.0))


def solution(mesh):
    placed = (
        P("dp", "cell"),
        P(None, "cell"),
        P("cell"),
        P("cell"),
        P("cell", None, None),
        P(None, "cell"),
    )
    return jax.shard_map(
        on_device, mesh=mesh, in_specs=placed, out_specs=P(None, "cell"), check_vma=False
    )
```

```python
import jax
import jax.numpy as jnp
from jax import lax
from jax.sharding import PartitionSpec as P


def padded_2(value, sides, width):
    for axis, dim in sides:
        count, length = (lax.axis_size(axis), value.shape[dim])
        up = [(i, (i + 1) % count) for i in range(count - 1)]
        down = [(j, i) for i, j in up]
        last = lax.slice_in_dim(value, length - width, length, axis=dim)
        leading = lax.slice_in_dim(value, 0, width, axis=dim)
        before = lax.ppermute(last, axis, up)
        after = lax.ppermute(leading, axis, down)
        value = jnp.concatenate([before, value, after], axis=dim)
    return value


def butterfly_sum(value, axis):
    count = lax.axis_size(axis)
    step = 1
    while step < count:
        pairs = [(j, j ^ step) for j in range(count)]
        value = value + lax.ppermute(value, axis, pairs)
        step *= 2
    return value


def halving_sum(value, axis):
    count = lax.axis_size(axis)
    me = lax.axis_index(axis)
    steps = []
    step = 1
    while step < count:
        steps.append(step)
        step *= 2
    for step in steps:
        half = value.shape[0] // 2
        low, high = value[:half], value[half:]
        upper = (me & step) != 0
        keep = jnp.where(upper, high, low)
        send = jnp.where(upper, low, high)
        pairs = [(j, j ^ step) for j in range(count)]
        value = keep + lax.ppermute(send, axis, pairs)
    for step in reversed(steps):
        pairs = [(j, j ^ step) for j in range(count)]
        other = lax.ppermute(value, axis, pairs)
        upper = (me & step) != 0
        low = jnp.where(upper, other, value)
        high = jnp.where(upper, value, other)
        value = jnp.concatenate([low, high], axis=0)
    return value


def pick_block():
    block_len = 8
    for candidate in range(128, 7, -8):
        block_len = candidate
        break
    return block_len


def pick_group(block_count):
    group_len = 1
    for candidate in range(1, 9):
        if block_count % candidate == 0:
            group_len = candidate
    return group_len


def smoothness(masked_f, weight, send_lists, neighbours, width):
    slots = masked_f.shape[1]
    values = jnp.concatenate([masked_f * weight[None, :], weight[None, :]], axis=0)
    picked = jnp.take(values, send_lists[0].reshape(-1), axis=1)
    rim = picked.shape[1] // 2
    padded = padded_2(picked, (("cell", 1),), rim)
    rim_vals = jnp.concatenate([padded[:, :rim], padded[:, 3 * rim :]], axis=1)
    lanes = values.shape[0]
    high = lax.reduce_precision(values, exponent_bits=8, mantissa_bits=7)
    rest = values - high
    middle = lax.reduce_precision(rest, exponent_bits=8, mantissa_bits=7)
    low = rest - middle
    split = jnp.concatenate([high, middle, low], axis=0).astype(jnp.bfloat16)
    rim_high = lax.reduce_precision(rim_vals, exponent_bits=8, mantissa_bits=7)
    rim_rest = rim_vals - rim_high
    rim_middle = lax.reduce_precision(rim_rest, exponent_bits=8, mantissa_bits=7)
    rim_split = jnp.concatenate([rim_high, rim_middle, rim_rest - rim_middle], axis=0)
    rim_split = rim_split.astype(jnp.bfloat16)
    block_len = pick_block()
    block_count = width // block_len
    pieces = 1 + (128 + block_len - 1) // block_len
    spread = jnp.pad(split, ((0, 0), (64, pieces * block_len)))
    local_vals = lax.slice_in_dim(spread, 0, (block_count + pieces - 1) * block_len, axis=1)
    shifted = [
        local_vals[:, m * block_len : (m + block_count) * block_len].reshape(
            3 * lanes, block_count, block_len
        )
        for m in range(pieces)
    ]
    rim_part = jnp.broadcast_to(rim_split[:, None, :], (3 * lanes, block_count, 2 * rim))
    windows = jnp.concatenate(shifted + [rim_part], axis=2).transpose(1, 0, 2)
    span = windows.shape[2]
    position = jnp.arange(width, dtype=jnp.int32)
    anchor = position // block_len * block_len
    column = jnp.where(
        neighbours < slots,
        neighbours - anchor[None, :] + 64,
        jnp.where(neighbours < slots + 2 * rim, pieces * block_len + neighbours - slots, -1),
    )
    column = column.reshape(neighbours.shape[0], block_count, block_len).transpose(1, 0, 2)
    group_len = pick_group(block_count)
    group_count = block_count // group_len
    sums = []
    for g in range(group_count):
        window_set = windows[g * group_len : (g + 1) * group_len]
        column_set = column[g * group_len : (g + 1) * group_len]
        target = jnp.arange(span, dtype=jnp.int32)[None, None, :, None]
        hits = jnp.sum(
            (column_set[:, :, None, :] == target).astype(jnp.bfloat16), axis=1, dtype=jnp.bfloat16
        )
        part = jnp.einsum(
            "grw,gwb->grb", window_set, hits, preferred_element_type=jnp.float32
        )
        sums.append(part[:, :lanes] + part[:, lanes : 2 * lanes] + part[:, 2 * lanes :])
    sums = jnp.concatenate(sums, axis=0)
    sums = sums.transpose(1, 0, 2).reshape(lanes, width)
    coupling = masked_f * sums[-1][None, :] - sums[:-1]
    return weight[None] * weight[None] * masked_f + weight[None] * coupling


def on_device(sensitivity, direction, depth_weight, counts, send_lists, neighbours):
    slots = sensitivity.shape[1]
    nvecs = direction.shape[0]
    live = jnp.arange(slots, dtype=jnp.int32) < counts[0]
    masked = jnp.where(live[None, :], direction, jnp.zeros_like(direction))
    partial_data = lax.dot_general(
        masked, sensitivity, (((1,), (1,)), ((), ())), preferred_element_type=jnp.float32
    )
    summed = butterfly_sum(partial_data, "cell")
    rounded = summed.astype(jnp.bfloat16)
    remainder = (summed - rounded.astype(jnp.float32)).astype(jnp.bfloat16)
    stacked = jnp.concatenate([rounded, remainder], axis=0)
    both = jnp.dot(stacked, sensitivity, preferred_element_type=jnp.float32)
    partial_cells = both[:nvecs] + both[nvecs:]
    weight = jnp.where(live, depth_weight, jnp.float32(0.0))
    masked_f = masked.astype(jnp.float32)
    misfit = halving_sum(partial_cells, "dp")
    smooth = smoothness(masked_f, weight, send_lists, neighbours, slots)
    total = misfit + 0.5 * smooth
    return jnp.where(live[None, :], total, jnp.float32(0.0))


def solution(mesh):
    placed = (
        P("dp", "cell"),
        P(None, "cell"),
        P("cell"),
        P("cell"),
        P("cell", None, None),
        P(None, "cell"),
    )
    return jax.shard_map(
        on_device, mesh=mesh, in_specs=placed, out_specs=P(None, "cell"), check_vma=False
    )
```

```python
import jax
import jax.numpy as jnp
from jax import lax
from jax.sharding import PartitionSpec as P


def padded_2(value, sides, width):
    for axis, dim in sides:
        count, length = (lax.axis_size(axis), value.shape[dim])
        up = [(i, (i + 1) % count) for i in range(count - 1)]
        down = [(j, i) for i, j in up]
        last = lax.slice_in_dim(value, length - width, length, axis=dim)
        leading = lax.slice_in_dim(value, 0, width, axis=dim)
        before = lax.ppermute(last, axis, up)
        after = lax.ppermute(leading, axis, down)
        value = jnp.concatenate([before, value, after], axis=dim)
    return value


def butterfly_sum(value, axis):
    count = lax.axis_size(axis)
    step = 1
    while step < count:
        pairs = [(j, j ^ step) for j in range(count)]
        value = value + lax.ppermute(value, axis, pairs)
        step *= 2
    return value


def halving_sum(value, axis):
    count = lax.axis_size(axis)
    me = lax.axis_index(axis)
    steps = []
    step = 1
    while step < count:
        steps.append(step)
        step *= 2
    for step in steps:
        half = value.shape[0] // 2
        low, high = value[:half], value[half:]
        upper = (me & step) != 0
        keep = jnp.where(upper, high, low)
        send = jnp.where(upper, low, high)
        pairs = [(j, j ^ step) for j in range(count)]
        value = keep + lax.ppermute(send, axis, pairs)
    for step in reversed(steps):
        pairs = [(j, j ^ step) for j in range(count)]
        other = lax.ppermute(value, axis, pairs)
        upper = (me & step) != 0
        low = jnp.where(upper, other, value)
        high = jnp.where(upper, value, other)
        value = jnp.concatenate([low, high], axis=0)
    return value


def exchange_sum(value, axis):
    count = lax.axis_size(axis)
    rows = value.shape[0] // count
    pieces = value.reshape(count, rows, value.shape[1])
    pieces = lax.all_to_all(pieces, axis, 0, 0)
    total = pieces[0]
    for source in range(1, count):
        total = total + pieces[source]
    return lax.all_gather(total, axis, axis=0, tiled=True)


def pick_block():
    block_len = 8
    for candidate in range(128, 7, -8):
        block_len = candidate
        break
    return block_len


def pick_group(block_count):
    group_len = 1
    for candidate in range(1, 9):
        if block_count % candidate == 0:
            group_len = candidate
    return group_len


def smoothness(masked_f, weight, send_lists, neighbours, width):
    slots = masked_f.shape[1]
    values = jnp.concatenate([masked_f * weight[None, :], weight[None, :]], axis=0)
    picked = jnp.take(values, send_lists[0].reshape(-1), axis=1)
    rim = picked.shape[1] // 2
    padded = padded_2(picked, (("cell", 1),), rim)
    rim_vals = jnp.concatenate([padded[:, :rim], padded[:, 3 * rim :]], axis=1)
    lanes = values.shape[0]
    high = lax.reduce_precision(values, exponent_bits=8, mantissa_bits=7)
    rest = values - high
    middle = lax.reduce_precision(rest, exponent_bits=8, mantissa_bits=7)
    low = rest - middle
    split = jnp.concatenate([high, middle, low], axis=0).astype(jnp.bfloat16)
    rim_high = lax.reduce_precision(rim_vals, exponent_bits=8, mantissa_bits=7)
    rim_rest = rim_vals - rim_high
    rim_middle = lax.reduce_precision(rim_rest, exponent_bits=8, mantissa_bits=7)
    rim_split = jnp.concatenate([rim_high, rim_middle, rim_rest - rim_middle], axis=0)
    rim_split = rim_split.astype(jnp.bfloat16)
    block_len = pick_block()
    block_count = width // block_len
    pieces = 1 + (128 + block_len - 1) // block_len
    spread = jnp.pad(split, ((0, 0), (64, pieces * block_len)))
    local_vals = lax.slice_in_dim(spread, 0, (block_count + pieces - 1) * block_len, axis=1)
    shifted = [
        local_vals[:, m * block_len : (m + block_count) * block_len].reshape(
            3 * lanes, block_count, block_len
        )
        for m in range(pieces)
    ]
    rim_part = jnp.broadcast_to(rim_split[:, None, :], (3 * lanes, block_count, 2 * rim))
    windows = jnp.concatenate(shifted + [rim_part], axis=2).transpose(1, 0, 2)
    span = windows.shape[2]
    position = jnp.arange(width, dtype=jnp.int32)
    anchor = position // block_len * block_len
    column = jnp.where(
        neighbours < slots,
        neighbours - anchor[None, :] + 64,
        jnp.where(neighbours < slots + 2 * rim, pieces * block_len + neighbours - slots, -1),
    )
    column = column.reshape(neighbours.shape[0], block_count, block_len).transpose(1, 0, 2)
    group_len = pick_group(block_count)
    group_count = block_count // group_len
    sums = []
    for g in range(group_count):
        window_set = windows[g * group_len : (g + 1) * group_len]
        column_set = column[g * group_len : (g + 1) * group_len]
        target = jnp.arange(span, dtype=jnp.int32)[None, None, :, None]
        hits = jnp.sum((column_set[:, :, None, :] == target).astype(jnp.float32), axis=1)
        hits = hits.astype(jnp.bfloat16)
        part = jnp.einsum(
            "grw,gwb->grb", window_set, hits, preferred_element_type=jnp.float32
        )
        sums.append(part[:, :lanes] + part[:, lanes : 2 * lanes] + part[:, 2 * lanes :])
    sums = jnp.concatenate(sums, axis=0)
    sums = sums.transpose(1, 0, 2).reshape(lanes, width)
    coupling = masked_f * sums[-1][None, :] - sums[:-1]
    return weight[None] * weight[None] * masked_f + weight[None] * coupling


def on_device(sensitivity, direction, depth_weight, counts, send_lists, neighbours):
    slots = sensitivity.shape[1]
    nvecs = direction.shape[0]
    live = jnp.arange(slots, dtype=jnp.int32) < counts[0]
    masked = jnp.where(live[None, :], direction, jnp.zeros_like(direction))
    partial_data = lax.dot_general(
        masked, sensitivity, (((1,), (1,)), ((), ())), preferred_element_type=jnp.float32
    )
    summed = butterfly_sum(partial_data, "cell")
    rounded = summed.astype(jnp.bfloat16)
    remainder = (summed - rounded.astype(jnp.float32)).astype(jnp.bfloat16)
    stacked = jnp.concatenate([rounded, remainder], axis=0)
    both = jnp.dot(stacked, sensitivity, preferred_element_type=jnp.float32)
    partial_cells = both[:nvecs] + both[nvecs:]
    weight = jnp.where(live, depth_weight, jnp.float32(0.0))
    masked_f = masked.astype(jnp.float32)
    misfit = exchange_sum(partial_cells, "dp")
    smooth = smoothness(masked_f, weight, send_lists, neighbours, slots)
    total = misfit + 0.5 * smooth
    return jnp.where(live[None, :], total, jnp.float32(0.0))


def solution(mesh):
    placed = (
        P("dp", "cell"),
        P(None, "cell"),
        P("cell"),
        P("cell"),
        P("cell", None, None),
        P(None, "cell"),
    )
    return jax.shard_map(
        on_device, mesh=mesh, in_specs=placed, out_specs=P(None, "cell"), check_vma=False
    )
```

```python
import jax
import jax.numpy as jnp
from jax import lax
from jax.sharding import PartitionSpec as P


def padded_2(value, sides, width):
    for axis, dim in sides:
        count, length = (lax.axis_size(axis), value.shape[dim])
        up = [(i, (i + 1) % count) for i in range(count - 1)]
        down = [(j, i) for i, j in up]
        last = lax.slice_in_dim(value, length - width, length, axis=dim)
        leading = lax.slice_in_dim(value, 0, width, axis=dim)
        before = lax.ppermute(last, axis, up)
        after = lax.ppermute(leading, axis, down)
        value = jnp.concatenate([before, value, after], axis=dim)
    return value


def butterfly_sum(value, axis):
    count = lax.axis_size(axis)
    rounds = []
    step = 1
    while step < count:
        pairs = [(j, j ^ step) for j in range(count)]
        value = value + lax.ppermute(value, axis, pairs)
        rounds.append(value)
        step *= 2
    return value, rounds


def halving_sum(value, axis):
    count = lax.axis_size(axis)
    me = lax.axis_index(axis)
    steps = []
    step = 1
    while step < count:
        steps.append(step)
        step *= 2
    for step in steps:
        half = value.shape[0] // 2
        low, high = value[:half], value[half:]
        upper = (me & step) != 0
        keep = jnp.where(upper, high, low)
        send = jnp.where(upper, low, high)
        pairs = [(j, j ^ step) for j in range(count)]
        value = keep + lax.ppermute(send, axis, pairs)
    for step in reversed(steps):
        pairs = [(j, j ^ step) for j in range(count)]
        other = lax.ppermute(value, axis, pairs)
        upper = (me & step) != 0
        low = jnp.where(upper, other, value)
        high = jnp.where(upper, value, other)
        value = jnp.concatenate([low, high], axis=0)
    return value


def exchange_sum(value, axis):
    count = lax.axis_size(axis)
    rows = value.shape[0] // count
    pieces = value.reshape(count, rows, value.shape[1])
    pieces = lax.all_to_all(pieces, axis, 0, 0)
    total = pieces[0]
    for source in range(1, count):
        total = total + pieces[source]
    return lax.all_gather(total, axis, axis=0, tiled=True)


def pick_block():
    block_len = 8
    for candidate in range(128, 7, -8):
        block_len = candidate
        break
    return block_len


def pick_group(block_count):
    group_len = 1
    for candidate in range(1, 9):
        if block_count % candidate == 0:
            group_len = candidate
    return group_len


def smoothness(masked_f, weight, send_lists, neighbours, width, gates):
    slots = masked_f.shape[1]
    values = jnp.concatenate([masked_f * weight[None, :], weight[None, :]], axis=0)
    rim_index, _ = lax.optimization_barrier((send_lists[0], gates[0]))
    picked = jnp.take(values, rim_index.reshape(-1), axis=1)
    rim = picked.shape[1] // 2
    padded = padded_2(picked, (("cell", 1),), rim)
    rim_vals = jnp.concatenate([padded[:, :rim], padded[:, 3 * rim :]], axis=1)
    lanes = values.shape[0]
    high = lax.reduce_precision(values, exponent_bits=8, mantissa_bits=7)
    rest = values - high
    middle = lax.reduce_precision(rest, exponent_bits=8, mantissa_bits=7)
    low = rest - middle
    split = jnp.concatenate([high, middle, low], axis=0).astype(jnp.bfloat16)
    rim_high = lax.reduce_precision(rim_vals, exponent_bits=8, mantissa_bits=7)
    rim_rest = rim_vals - rim_high
    rim_middle = lax.reduce_precision(rim_rest, exponent_bits=8, mantissa_bits=7)
    rim_split = jnp.concatenate([rim_high, rim_middle, rim_rest - rim_middle], axis=0)
    rim_split = rim_split.astype(jnp.bfloat16)
    block_len = pick_block()
    block_count = width // block_len
    pieces = 1 + (128 + block_len - 1) // block_len
    spread = jnp.pad(split, ((0, 0), (64, pieces * block_len)))
    local_vals = lax.slice_in_dim(spread, 0, (block_count + pieces - 1) * block_len, axis=1)
    shifted = [
        local_vals[:, m * block_len : (m + block_count) * block_len].reshape(
            3 * lanes, block_count, block_len
        )
        for m in range(pieces)
    ]
    rim_part = jnp.broadcast_to(rim_split[:, None, :], (3 * lanes, block_count, 2 * rim))
    windows = jnp.concatenate(shifted + [rim_part], axis=2).transpose(1, 0, 2)
    span = windows.shape[2]
    position = jnp.arange(width, dtype=jnp.int32)
    anchor = position // block_len * block_len
    column = jnp.where(
        neighbours < slots,
        neighbours - anchor[None, :] + 64,
        jnp.where(neighbours < slots + 2 * rim, pieces * block_len + neighbours - slots, -1),
    )
    column = column.reshape(neighbours.shape[0], block_count, block_len).transpose(1, 0, 2)
    group_len = pick_group(block_count)
    group_count = block_count // group_len
    sums = []
    for g in range(group_count):
        window_set = windows[g * group_len : (g + 1) * group_len]
        column_set = column[g * group_len : (g + 1) * group_len]
        gate = gates[min(g, len(gates) - 1)]
        target = jnp.arange(span, dtype=jnp.int32)[None, None, :, None]
        column_set, _ = lax.optimization_barrier((column_set, gate))
        hits = jnp.sum((column_set[:, :, None, :] == target).astype(jnp.float32), axis=1)
        hits = hits.astype(jnp.bfloat16)
        part = jnp.einsum(
            "grw,gwb->grb", window_set, hits, preferred_element_type=jnp.float32
        )
        sums.append(part[:, :lanes] + part[:, lanes : 2 * lanes] + part[:, 2 * lanes :])
    sums = jnp.concatenate(sums, axis=0)
    sums = sums.transpose(1, 0, 2).reshape(lanes, width)
    coupling = masked_f * sums[-1][None, :] - sums[:-1]
    return weight[None] * weight[None] * masked_f + weight[None] * coupling


def on_device(sensitivity, direction, depth_weight, counts, send_lists, neighbours):
    slots = sensitivity.shape[1]
    nvecs = direction.shape[0]
    live = jnp.arange(slots, dtype=jnp.int32) < counts[0]
    masked = jnp.where(live[None, :], direction, jnp.zeros_like(direction))
    partial_data = lax.dot_general(
        masked, sensitivity, (((1,), (1,)), ((), ())), preferred_element_type=jnp.float32
    )
    summed, rounds = butterfly_sum(partial_data, "cell")
    rounded = summed.astype(jnp.bfloat16)
    remainder = (summed - rounded.astype(jnp.float32)).astype(jnp.bfloat16)
    stacked = jnp.concatenate([rounded, remainder], axis=0)
    both = jnp.dot(stacked, sensitivity, preferred_element_type=jnp.float32)
    partial_cells = both[:nvecs] + both[nvecs:]
    weight = jnp.where(live, depth_weight, jnp.float32(0.0))
    masked_f = masked.astype(jnp.float32)
    misfit = exchange_sum(partial_cells, "dp")
    gates = rounds[:-1] + [partial_cells]
    smooth = smoothness(masked_f, weight, send_lists, neighbours, slots, gates)
    total = misfit + 0.5 * smooth
    return jnp.where(live[None, :], total, jnp.float32(0.0))


def solution(mesh):
    placed = (
        P("dp", "cell"),
        P(None, "cell"),
        P("cell"),
        P("cell"),
        P("cell", None, None),
        P(None, "cell"),
    )
    return jax.shard_map(
        on_device, mesh=mesh, in_specs=placed, out_specs=P(None, "cell"), check_vma=False
    )
```

```python
import jax
import jax.numpy as jnp
from jax import lax
from jax.sharding import PartitionSpec as P


def padded_2(value, sides, width):
    for axis, dim in sides:
        count, length = (lax.axis_size(axis), value.shape[dim])
        up = [(i, (i + 1) % count) for i in range(count - 1)]
        down = [(j, i) for i, j in up]
        last = lax.slice_in_dim(value, length - width, length, axis=dim)
        leading = lax.slice_in_dim(value, 0, width, axis=dim)
        before = lax.ppermute(last, axis, up)
        after = lax.ppermute(leading, axis, down)
        value = jnp.concatenate([before, value, after], axis=dim)
    return value


def butterfly_sum(value, axis):
    count = lax.axis_size(axis)
    rounds = []
    step = 1
    while step < count:
        pairs = [(j, j ^ step) for j in range(count)]
        value = value + lax.ppermute(value, axis, pairs)
        rounds.append(value)
        step *= 2
    return value, rounds


def exchange_sum(value, axis):
    count = lax.axis_size(axis)
    rows = value.shape[0] // count
    pieces = value.reshape(count, rows, value.shape[1])
    pieces = lax.all_to_all(pieces, axis, 0, 0)
    total = pieces[0]
    for source in range(1, count):
        total = total + pieces[source]
    return lax.all_gather(total, axis, axis=0, tiled=True)


def pick_block():
    block_len = 8
    for candidate in range(128, 7, -8):
        block_len = candidate
        break
    return block_len


def pick_group(block_count):
    group_len = 1
    for candidate in range(1, 9):
        if block_count % candidate == 0:
            group_len = candidate
    return group_len


def smoothness(masked_f, weight, send_lists, neighbours, width, gates):
    slots = masked_f.shape[1]
    values = jnp.concatenate([masked_f * weight[None, :], weight[None, :]], axis=0)
    lanes = values.shape[0]
    high = lax.reduce_precision(values, exponent_bits=8, mantissa_bits=7)
    rest = values - high
    middle = lax.reduce_precision(rest, exponent_bits=8, mantissa_bits=7)
    low = rest - middle
    split = jnp.concatenate([high, middle, low], axis=0).astype(jnp.bfloat16)
    rim_index, _ = lax.optimization_barrier((send_lists[0], gates[0]))
    chosen = jnp.arange(slots, dtype=jnp.int32)[:, None] == rim_index.reshape(1, -1)
    chosen_parts = jnp.dot(split, chosen.astype(jnp.bfloat16), preferred_element_type=jnp.float32)
    picked = chosen_parts[:lanes] + chosen_parts[lanes : 2 * lanes] + chosen_parts[2 * lanes :]
    rim = picked.shape[1] // 2
    padded = padded_2(picked, (("cell", 1),), rim)
    rim_vals = jnp.concatenate([padded[:, :rim], padded[:, 3 * rim :]], axis=1)
    rim_high = lax.reduce_precision(rim_vals, exponent_bits=8, mantissa_bits=7)
    rim_rest = rim_vals - rim_high
    rim_middle = lax.reduce_precision(rim_rest, exponent_bits=8, mantissa_bits=7)
    rim_split = jnp.concatenate([rim_high, rim_middle, rim_rest - rim_middle], axis=0)
    rim_split = rim_split.astype(jnp.bfloat16)
    block_len = pick_block()
    block_count = width // block_len
    pieces = 1 + (128 + block_len - 1) // block_len
    spread = jnp.pad(split, ((0, 0), (64, pieces * block_len)))
    local_vals = lax.slice_in_dim(spread, 0, (block_count + pieces - 1) * block_len, axis=1)
    shifted = [
        local_vals[:, m * block_len : (m + block_count) * block_len].reshape(
            3 * lanes, block_count, block_len
        )
        for m in range(pieces)
    ]
    rim_part = jnp.broadcast_to(rim_split[:, None, :], (3 * lanes, block_count, 2 * rim))
    windows = jnp.concatenate(shifted + [rim_part], axis=2).transpose(1, 0, 2)
    span = windows.shape[2]
    position = jnp.arange(width, dtype=jnp.int32)
    anchor = position // block_len * block_len
    column = jnp.where(
        neighbours < slots,
        neighbours - anchor[None, :] + 64,
        jnp.where(neighbours < slots + 2 * rim, pieces * block_len + neighbours - slots, -1),
    )
    column = column.reshape(neighbours.shape[0], block_count, block_len).transpose(1, 0, 2)
    group_len = pick_group(block_count)
    group_count = block_count // group_len
    sums = []
    for g in range(group_count):
        window_set = windows[g * group_len : (g + 1) * group_len]
        column_set = column[g * group_len : (g + 1) * group_len]
        gate = gates[min(g, len(gates) - 1)]
        target = jnp.arange(span, dtype=jnp.int32)[None, None, :, None]
        column_set, _ = lax.optimization_barrier((column_set, gate))
        hits = jnp.sum((column_set[:, :, None, :] == target).astype(jnp.float32), axis=1)
        hits = hits.astype(jnp.bfloat16)
        part = jnp.einsum(
            "grw,gwb->grb", window_set, hits, preferred_element_type=jnp.float32
        )
        sums.append(part[:, :lanes] + part[:, lanes : 2 * lanes] + part[:, 2 * lanes :])
    sums = jnp.concatenate(sums, axis=0)
    sums = sums.transpose(1, 0, 2).reshape(lanes, width)
    coupling = masked_f * sums[-1][None, :] - sums[:-1]
    return weight[None] * weight[None] * masked_f + weight[None] * coupling


def on_device_body(sensitivity, direction, depth_weight, counts, send_lists, neighbours):
    slots = sensitivity.shape[1]
    nvecs = direction.shape[0]
    live = jnp.arange(slots, dtype=jnp.int32) < counts[0]
    masked = jnp.where(live[None, :], direction, jnp.zeros_like(direction))
    partial_data = lax.dot_general(
        masked, sensitivity, (((1,), (1,)), ((), ())), preferred_element_type=jnp.float32
    )
    summed, rounds = butterfly_sum(partial_data, "cell")
    rounded = summed.astype(jnp.bfloat16)
    remainder = (summed - rounded.astype(jnp.float32)).astype(jnp.bfloat16)
    stacked = jnp.concatenate([rounded, remainder], axis=0)
    both = jnp.dot(stacked, sensitivity, preferred_element_type=jnp.float32)
    partial_cells = both[:nvecs] + both[nvecs:]
    weight = jnp.where(live, depth_weight, jnp.float32(0.0))
    masked_f = masked.astype(jnp.float32)
    misfit = exchange_sum(partial_cells, "dp")
    gates = rounds[:-1] + [partial_cells]
    smooth = smoothness(masked_f, weight, send_lists, neighbours, slots, gates)
    total = misfit + 0.5 * smooth
    return jnp.where(live[None, :], total, jnp.float32(0.0))


def solution(mesh):
    placed = (
        P("dp", "cell"),
        P(None, "cell"),
        P("cell"),
        P("cell"),
        P("cell", None, None),
        P(None, "cell"),
    )
    return jax.shard_map(
        on_device_body, mesh=mesh, in_specs=placed, out_specs=P(None, "cell"), check_vma=False
    )
```

```python
import jax
import jax.numpy as jnp
from jax import lax
from jax.sharding import Mesh, PartitionSpec as P


def padded_2(value, sides, width):
    for axis, dim in sides:
        count, length = (lax.axis_size(axis), value.shape[dim])
        up = [(i, (i + 1) % count) for i in range(count - 1)]
        down = [(j, i) for i, j in up]
        last = lax.slice_in_dim(value, length - width, length, axis=dim)
        leading = lax.slice_in_dim(value, 0, width, axis=dim)
        before = lax.ppermute(last, axis, up)
        after = lax.ppermute(leading, axis, down)
        value = jnp.concatenate([before, value, after], axis=dim)
    return value


def exchange_sum(value, axis):
    count = lax.axis_size(axis)
    rows = value.shape[0] // count
    pieces = value.reshape(count, rows, value.shape[1])
    pieces = lax.all_to_all(pieces, axis, 0, 0)
    total = pieces[0]
    for source in range(1, count):
        total = total + pieces[source]
    return lax.all_gather(total, axis, axis=0, tiled=True)


def pick_block():
    block_len = 8
    for candidate in range(128, 7, -8):
        block_len = candidate
        break
    return block_len


def pick_group(block_count):
    group_len = 1
    for candidate in range(1, 9):
        if block_count % candidate == 0:
            group_len = candidate
    return group_len


def smoothness(masked_f, weight, send_lists, neighbours, width, gates):
    slots = masked_f.shape[1]
    values = jnp.concatenate([masked_f * weight[None, :], weight[None, :]], axis=0)
    lanes = values.shape[0]
    high = lax.reduce_precision(values, exponent_bits=8, mantissa_bits=7)
    rest = values - high
    middle = lax.reduce_precision(rest, exponent_bits=8, mantissa_bits=7)
    low = rest - middle
    split = jnp.concatenate([high, middle, low], axis=0).astype(jnp.bfloat16)
    rim_index, _ = lax.optimization_barrier((send_lists[0], gates[0]))
    chosen = jnp.arange(slots, dtype=jnp.int32)[:, None] == rim_index.reshape(1, -1)
    chosen_parts = jnp.dot(split, chosen.astype(jnp.bfloat16), preferred_element_type=jnp.float32)
    picked = chosen_parts[:lanes] + chosen_parts[lanes : 2 * lanes] + chosen_parts[2 * lanes :]
    rim = picked.shape[1] // 2
    padded = padded_2(picked, ((CELL, 1),), rim)
    rim_vals = jnp.concatenate([padded[:, :rim], padded[:, 3 * rim :]], axis=1)
    rim_high = lax.reduce_precision(rim_vals, exponent_bits=8, mantissa_bits=7)
    rim_rest = rim_vals - rim_high
    rim_middle = lax.reduce_precision(rim_rest, exponent_bits=8, mantissa_bits=7)
    rim_split = jnp.concatenate([rim_high, rim_middle, rim_rest - rim_middle], axis=0)
    rim_split = rim_split.astype(jnp.bfloat16)
    block_len = pick_block()
    block_count = width // block_len
    pieces = 1 + (128 + block_len - 1) // block_len
    spread = jnp.pad(split, ((0, 0), (64, pieces * block_len)))
    local_vals = lax.slice_in_dim(spread, 0, (block_count + pieces - 1) * block_len, axis=1)
    shifted = [
        local_vals[:, m * block_len : (m + block_count) * block_len].reshape(
            3 * lanes, block_count, block_len
        )
        for m in range(pieces)
    ]
    rim_part = jnp.broadcast_to(rim_split[:, None, :], (3 * lanes, block_count, 2 * rim))
    windows = jnp.concatenate(shifted + [rim_part], axis=2).transpose(1, 0, 2)
    span = windows.shape[2]
    position = jnp.arange(width, dtype=jnp.int32)
    anchor = position // block_len * block_len
    column = jnp.where(
        neighbours < slots,
        neighbours - anchor[None, :] + 64,
        jnp.where(neighbours < slots + 2 * rim, pieces * block_len + neighbours - slots, -1),
    )
    column = column.reshape(neighbours.shape[0], block_count, block_len).transpose(1, 0, 2)
    group_len = pick_group(block_count)
    group_count = block_count // group_len
    sums = []
    for g in range(group_count):
        window_set = windows[g * group_len : (g + 1) * group_len]
        column_set = column[g * group_len : (g + 1) * group_len]
        gate = gates[min(g, len(gates) - 1)]
        target = jnp.arange(span, dtype=jnp.int32)[None, None, :, None]
        column_set, _ = lax.optimization_barrier((column_set, gate))
        hits = jnp.sum((column_set[:, :, None, :] == target).astype(jnp.float32), axis=1)
        hits = hits.astype(jnp.bfloat16)
        part = jnp.einsum(
            "grw,gwb->grb", window_set, hits, preferred_element_type=jnp.float32
        )
        sums.append(part[:, :lanes] + part[:, lanes : 2 * lanes] + part[:, 2 * lanes :])
    sums = jnp.concatenate(sums, axis=0)
    sums = sums.transpose(1, 0, 2).reshape(lanes, width)
    coupling = masked_f * sums[-1][None, :] - sums[:-1]
    return weight[None] * weight[None] * masked_f + weight[None] * coupling


def on_device_body(sensitivity, direction, depth_weight, counts, send_lists, neighbours):
    slots = sensitivity.shape[1]
    nvecs = direction.shape[0]
    live = jnp.arange(slots, dtype=jnp.int32) < counts[0]
    masked = jnp.where(live[None, :], direction, jnp.zeros_like(direction))
    partial_data = lax.dot_general(
        masked, sensitivity, (((1,), (1,)), ((), ())), preferred_element_type=jnp.float32
    )
    summed = lax.psum(lax.psum(partial_data, "z"), "x")
    rounded = summed.astype(jnp.bfloat16)
    remainder = (summed - rounded.astype(jnp.float32)).astype(jnp.bfloat16)
    stacked = jnp.concatenate([rounded, remainder], axis=0)
    both = jnp.dot(stacked, sensitivity, preferred_element_type=jnp.float32)
    partial_cells = both[:nvecs] + both[nvecs:]
    weight = jnp.where(live, depth_weight, jnp.float32(0.0))
    masked_f = masked.astype(jnp.float32)
    misfit = exchange_sum(partial_cells, DP)
    gates = [partial_cells]
    smooth = smoothness(masked_f, weight, send_lists, neighbours, slots, gates)
    total = misfit + 0.5 * smooth
    return jnp.where(live[None, :], total, jnp.float32(0.0))


DP = ("y", "core")
CELL = ("x", "z")


def solution(mesh):
    dp_size, cell_size = mesh.devices.shape
    z_size = 8 if cell_size % 8 == 0 else cell_size
    split_mesh = Mesh(
        mesh.devices.reshape(dp_size // 2, 2, cell_size // z_size, z_size), DP + CELL
    )
    placed = (
        P(DP, CELL),
        P(None, CELL),
        P(CELL),
        P(CELL),
        P(CELL, None, None),
        P(None, CELL),
    )
    return jax.shard_map(
        on_device_body, mesh=split_mesh, in_specs=placed, out_specs=P(None, CELL), check_vma=False
    )
```

```python
import jax
import jax.numpy as jnp
from jax import lax
from jax.sharding import Mesh, PartitionSpec as P


def padded_2(value, sides, width):
    for axis, dim in sides:
        count, length = (lax.axis_size(axis), value.shape[dim])
        up = [(i, (i + 1) % count) for i in range(count - 1)]
        down = [(j, i) for i, j in up]
        last = lax.slice_in_dim(value, length - width, length, axis=dim)
        leading = lax.slice_in_dim(value, 0, width, axis=dim)
        before = lax.ppermute(last, axis, up)
        after = lax.ppermute(leading, axis, down)
        value = jnp.concatenate([before, value, after], axis=dim)
    return value


def butterfly_sum(value, axis):
    count = lax.axis_size(axis)
    rounds = []
    step = 1
    while step < count:
        pairs = [(j, j ^ step) for j in range(count)]
        value = value + lax.ppermute(value, axis, pairs)
        rounds.append(value)
        step *= 2
    return value, rounds


def exchange_sum(value, axis):
    count = lax.axis_size(axis)
    rows = value.shape[0] // count
    pieces = value.reshape(count, rows, value.shape[1])
    pieces = lax.all_to_all(pieces, axis, 0, 0)
    total = pieces[0]
    for source in range(1, count):
        total = total + pieces[source]
    return lax.all_gather(total, axis, axis=0, tiled=True)


def pick_block():
    block_len = 8
    for candidate in range(128, 7, -8):
        block_len = candidate
        break
    return block_len


def pick_group(block_count):
    group_len = 1
    for candidate in range(1, 9):
        if block_count % candidate == 0:
            group_len = candidate
    return group_len


def smoothness(masked_f, weight, send_lists, neighbours, width, gates):
    slots = masked_f.shape[1]
    values = jnp.concatenate([masked_f * weight[None, :], weight[None, :]], axis=0)
    values, _ = lax.optimization_barrier((values, gates[0]))
    lanes = values.shape[0]
    high = lax.reduce_precision(values, exponent_bits=8, mantissa_bits=7)
    rest = values - high
    middle = lax.reduce_precision(rest, exponent_bits=8, mantissa_bits=7)
    low = rest - middle
    split = jnp.concatenate([high, middle, low], axis=0).astype(jnp.bfloat16)
    rim_index, _ = lax.optimization_barrier((send_lists[0], gates[0]))
    chosen = jnp.arange(slots, dtype=jnp.int32)[:, None] == rim_index.reshape(1, -1)
    chosen_parts = jnp.dot(split, chosen.astype(jnp.bfloat16), preferred_element_type=jnp.float32)
    picked = chosen_parts[:lanes] + chosen_parts[lanes : 2 * lanes] + chosen_parts[2 * lanes :]
    rim = picked.shape[1] // 2
    padded = padded_2(picked, ((CELL, 1),), rim)
    rim_vals = jnp.concatenate([padded[:, :rim], padded[:, 3 * rim :]], axis=1)
    rim_high = lax.reduce_precision(rim_vals, exponent_bits=8, mantissa_bits=7)
    rim_rest = rim_vals - rim_high
    rim_middle = lax.reduce_precision(rim_rest, exponent_bits=8, mantissa_bits=7)
    rim_split = jnp.concatenate([rim_high, rim_middle, rim_rest - rim_middle], axis=0)
    rim_split = rim_split.astype(jnp.bfloat16)
    block_len = pick_block()
    block_count = width // block_len
    pieces = 1 + (128 + block_len - 1) // block_len
    spread = jnp.pad(split, ((0, 0), (64, pieces * block_len)))
    local_vals = lax.slice_in_dim(spread, 0, (block_count + pieces - 1) * block_len, axis=1)
    shifted = [
        local_vals[:, m * block_len : (m + block_count) * block_len].reshape(
            3 * lanes, block_count, block_len
        )
        for m in range(pieces)
    ]
    rim_part = jnp.broadcast_to(rim_split[:, None, :], (3 * lanes, block_count, 2 * rim))
    windows = jnp.concatenate(shifted + [rim_part], axis=2).transpose(1, 0, 2)
    span = windows.shape[2]
    position = jnp.arange(width, dtype=jnp.int32)
    anchor = position // block_len * block_len
    column = jnp.where(
        neighbours < slots,
        neighbours - anchor[None, :] + 64,
        jnp.where(neighbours < slots + 2 * rim, pieces * block_len + neighbours - slots, -1),
    )
    column = column.reshape(neighbours.shape[0], block_count, block_len).transpose(1, 0, 2)
    group_len = pick_group(block_count)
    group_count = block_count // group_len
    sums = []
    for g in range(group_count):
        window_set = windows[g * group_len : (g + 1) * group_len]
        column_set = column[g * group_len : (g + 1) * group_len]
        gate = gates[min(g, len(gates) - 1)]
        target = jnp.arange(span, dtype=jnp.int32)[None, None, :, None]
        column_set, _ = lax.optimization_barrier((column_set, gate))
        hits = jnp.sum((column_set[:, :, None, :] == target).astype(jnp.float32), axis=1)
        hits = hits.astype(jnp.bfloat16)
        part = jnp.einsum(
            "grw,gwb->grb", window_set, hits, preferred_element_type=jnp.float32
        )
        sums.append(part[:, :lanes] + part[:, lanes : 2 * lanes] + part[:, 2 * lanes :])
    sums = jnp.concatenate(sums, axis=0)
    sums = sums.transpose(1, 0, 2).reshape(lanes, width)
    coupling = masked_f * sums[-1][None, :] - sums[:-1]
    return weight[None] * weight[None] * masked_f + weight[None] * coupling


def on_device_body(sensitivity, direction, depth_weight, counts, send_lists, neighbours):
    slots = sensitivity.shape[1]
    nvecs = direction.shape[0]
    live = jnp.arange(slots, dtype=jnp.int32) < counts[0]
    masked = jnp.where(live[None, :], direction, jnp.zeros_like(direction))
    partial_data = lax.dot_general(
        masked, sensitivity, (((1,), (1,)), ((), ())), preferred_element_type=jnp.float32
    )
    local_sum = lax.psum(partial_data, "z")
    summed, rounds = butterfly_sum(local_sum, "x")
    rounded = summed.astype(jnp.bfloat16)
    remainder = (summed - rounded.astype(jnp.float32)).astype(jnp.bfloat16)
    stacked = jnp.concatenate([rounded, remainder], axis=0)
    both = jnp.dot(stacked, sensitivity, preferred_element_type=jnp.float32)
    partial_cells = both[:nvecs] + both[nvecs:]
    weight = jnp.where(live, depth_weight, jnp.float32(0.0))
    masked_f = masked.astype(jnp.float32)
    misfit = exchange_sum(partial_cells, DP)
    gates = [local_sum, local_sum, rounds[0], rounds[0], partial_cells]
    smooth = smoothness(masked_f, weight, send_lists, neighbours, slots, gates)
    total = misfit + 0.5 * smooth
    return jnp.where(live[None, :], total, jnp.float32(0.0))


DP = ("y", "core")
CELL = ("x", "z")


def solution(mesh):
    dp_size, cell_size = mesh.devices.shape
    z_size = 8 if cell_size % 8 == 0 else cell_size
    split_mesh = Mesh(
        mesh.devices.reshape(dp_size // 2, 2, cell_size // z_size, z_size), DP + CELL
    )
    placed = (
        P(DP, CELL),
        P(None, CELL),
        P(CELL),
        P(CELL),
        P(CELL, None, None),
        P(None, CELL),
    )
    return jax.shard_map(
        on_device_body, mesh=split_mesh, in_specs=placed, out_specs=P(None, CELL), check_vma=False
    )
```

```python
import jax
import jax.numpy as jnp
from jax import lax
from jax.sharding import Mesh, PartitionSpec as P


def padded_2(value, sides, width):
    for axis, dim in sides:
        count, length = (lax.axis_size(axis), value.shape[dim])
        up = [(i, (i + 1) % count) for i in range(count - 1)]
        down = [(j, i) for i, j in up]
        last = lax.slice_in_dim(value, length - width, length, axis=dim)
        leading = lax.slice_in_dim(value, 0, width, axis=dim)
        before = lax.ppermute(last, axis, up)
        after = lax.ppermute(leading, axis, down)
        value = jnp.concatenate([before, value, after], axis=dim)
    return value


def butterfly_sum(value, axis):
    count = lax.axis_size(axis)
    rounds = []
    step = 1
    while step < count:
        pairs = [(j, j ^ step) for j in range(count)]
        value = value + lax.ppermute(value, axis, pairs)
        rounds.append(value)
        step *= 2
    return value, rounds


def exchange_sum(value, axis):
    count = lax.axis_size(axis)
    rows = value.shape[0] // count
    pieces = value.reshape(count, rows, value.shape[1])
    pieces = lax.all_to_all(pieces, axis, 0, 0)
    total = pieces[0]
    for source in range(1, count):
        total = total + pieces[source]
    for part in reversed(axis):
        total = lax.all_gather(total, part, axis=0, tiled=True)
    return total


def pick_block():
    block_len = 8
    for candidate in range(128, 7, -8):
        block_len = candidate
        break
    return block_len


def pick_group(block_count):
    group_len = 1
    for candidate in range(1, 9):
        if block_count % candidate == 0:
            group_len = candidate
    return group_len


def smoothness(masked_f, weight, send_lists, neighbours, width, gates):
    slots = masked_f.shape[1]
    values = jnp.concatenate([masked_f * weight[None, :], weight[None, :]], axis=0)
    lanes = values.shape[0]
    high = lax.reduce_precision(values, exponent_bits=8, mantissa_bits=7)
    rest = values - high
    middle = lax.reduce_precision(rest, exponent_bits=8, mantissa_bits=7)
    low = rest - middle
    split = jnp.concatenate([high, middle, low], axis=0).astype(jnp.bfloat16)
    rim_index, _ = lax.optimization_barrier((send_lists[0], gates[0]))
    chosen = jnp.arange(slots, dtype=jnp.int32)[:, None] == rim_index.reshape(1, -1)
    chosen_parts = jnp.dot(split, chosen.astype(jnp.bfloat16), preferred_element_type=jnp.float32)
    picked = chosen_parts[:lanes] + chosen_parts[lanes : 2 * lanes] + chosen_parts[2 * lanes :]
    rim = picked.shape[1] // 2
    padded = padded_2(picked, ((CELL, 1),), rim)
    rim_vals = jnp.concatenate([padded[:, :rim], padded[:, 3 * rim :]], axis=1)
    rim_high = lax.reduce_precision(rim_vals, exponent_bits=8, mantissa_bits=7)
    rim_rest = rim_vals - rim_high
    rim_middle = lax.reduce_precision(rim_rest, exponent_bits=8, mantissa_bits=7)
    rim_split = jnp.concatenate([rim_high, rim_middle, rim_rest - rim_middle], axis=0)
    rim_split = rim_split.astype(jnp.bfloat16)
    block_len = pick_block()
    block_count = width // block_len
    pieces = 1 + (128 + block_len - 1) // block_len
    spread = jnp.pad(split, ((0, 0), (64, pieces * block_len)))
    local_vals = lax.slice_in_dim(spread, 0, (block_count + pieces - 1) * block_len, axis=1)
    shifted = [
        local_vals[:, m * block_len : (m + block_count) * block_len].reshape(
            3 * lanes, block_count, block_len
        )
        for m in range(pieces)
    ]
    rim_part = jnp.broadcast_to(rim_split[:, None, :], (3 * lanes, block_count, 2 * rim))
    windows = jnp.concatenate(shifted + [rim_part], axis=2).transpose(1, 0, 2)
    span = windows.shape[2]
    position = jnp.arange(width, dtype=jnp.int32)
    anchor = position // block_len * block_len
    column = jnp.where(
        neighbours < slots,
        neighbours - anchor[None, :] + 64,
        jnp.where(neighbours < slots + 2 * rim, pieces * block_len + neighbours - slots, -1),
    )
    column = column.reshape(neighbours.shape[0], block_count, block_len).transpose(1, 0, 2)
    group_len = pick_group(block_count)
    group_count = block_count // group_len
    sums = []
    for g in range(group_count):
        window_set = windows[g * group_len : (g + 1) * group_len]
        column_set = column[g * group_len : (g + 1) * group_len]
        gate = gates[min(g, len(gates) - 1)]
        target = jnp.arange(span, dtype=jnp.int32)[None, None, :, None]
        column_set, _ = lax.optimization_barrier((column_set, gate))
        hits = jnp.sum((column_set[:, :, None, :] == target).astype(jnp.float32), axis=1)
        hits = hits.astype(jnp.bfloat16)
        part = jnp.einsum(
            "grw,gwb->grb", window_set, hits, preferred_element_type=jnp.float32
        )
        sums.append(part[:, :lanes] + part[:, lanes : 2 * lanes] + part[:, 2 * lanes :])
    sums = jnp.concatenate(sums, axis=0)
    sums = sums.transpose(1, 0, 2).reshape(lanes, width)
    coupling = masked_f * sums[-1][None, :] - sums[:-1]
    return weight[None] * weight[None] * masked_f + weight[None] * coupling


def on_device_body(sensitivity, direction, depth_weight, counts, send_lists, neighbours):
    slots = sensitivity.shape[1]
    nvecs = direction.shape[0]
    live = jnp.arange(slots, dtype=jnp.int32) < counts[0]
    masked = jnp.where(live[None, :], direction, jnp.zeros_like(direction))
    partial_data = lax.dot_general(
        masked, sensitivity, (((1,), (1,)), ((), ())), preferred_element_type=jnp.float32
    )
    summed, rounds = butterfly_sum(partial_data, CELL)
    rounded = summed.astype(jnp.bfloat16)
    remainder = (summed - rounded.astype(jnp.float32)).astype(jnp.bfloat16)
    stacked = jnp.concatenate([rounded, remainder], axis=0)
    both = jnp.dot(stacked, sensitivity, preferred_element_type=jnp.float32)
    partial_cells = both[:nvecs] + both[nvecs:]
    weight = jnp.where(live, depth_weight, jnp.float32(0.0))
    masked_f = masked.astype(jnp.float32)
    misfit = exchange_sum(partial_cells, DP)
    gates = rounds[:-1] + [partial_cells]
    smooth = smoothness(masked_f, weight, send_lists, neighbours, slots, gates)
    total = misfit + 0.5 * smooth
    return jnp.where(live[None, :], total, jnp.float32(0.0))


DP = ("y", "core")
CELL = ("x", "z")


def solution(mesh):
    dp_size, cell_size = mesh.devices.shape
    z_size = 8 if cell_size % 8 == 0 else cell_size
    split_mesh = Mesh(
        mesh.devices.reshape(dp_size // 2, 2, cell_size // z_size, z_size), DP + CELL
    )
    placed = (
        P(DP, CELL),
        P(None, CELL),
        P(CELL),
        P(CELL),
        P(CELL, None, None),
        P(None, CELL),
    )
    return jax.shard_map(
        on_device_body, mesh=split_mesh, in_specs=placed, out_specs=P(None, CELL), check_vma=False
    )
```

```python
import jax
import jax.numpy as jnp
from jax import lax
from jax.sharding import PartitionSpec as P


def padded_2(value, sides, width):
    for axis, dim in sides:
        count, length = (lax.axis_size(axis), value.shape[dim])
        up = [(i, (i + 1) % count) for i in range(count - 1)]
        down = [(j, i) for i, j in up]
        last = lax.slice_in_dim(value, length - width, length, axis=dim)
        leading = lax.slice_in_dim(value, 0, width, axis=dim)
        before = lax.ppermute(last, axis, up)
        after = lax.ppermute(leading, axis, down)
        value = jnp.concatenate([before, value, after], axis=dim)
    return value


def butterfly_sum(value, axis):
    count = lax.axis_size(axis)
    rounds = []
    step = 1
    while step < count:
        pairs = [(j, j ^ step) for j in range(count)]
        value = value + lax.ppermute(value, axis, pairs)
        rounds.append(value)
        step *= 2
    return value, rounds


def halving_sum(value, axis):
    count = lax.axis_size(axis)
    me = lax.axis_index(axis)
    steps = []
    step = 1
    while step < count:
        steps.append(step)
        step *= 2
    for step in steps:
        half = value.shape[0] // 2
        low, high = value[:half], value[half:]
        upper = (me & step) != 0
        keep = jnp.where(upper, high, low)
        send = jnp.where(upper, low, high)
        pairs = [(j, j ^ step) for j in range(count)]
        value = keep + lax.ppermute(send, axis, pairs)
    for step in reversed(steps):
        pairs = [(j, j ^ step) for j in range(count)]
        other = lax.ppermute(value, axis, pairs)
        upper = (me & step) != 0
        low = jnp.where(upper, other, value)
        high = jnp.where(upper, value, other)
        value = jnp.concatenate([low, high], axis=0)
    return value


def exchange_sum(value, axis):
    count = lax.axis_size(axis)
    rows = value.shape[0] // count
    pieces = value.reshape(count, rows, value.shape[1])
    pieces = lax.all_to_all(pieces, axis, 0, 0)
    total = pieces[0]
    for source in range(1, count):
        total = total + pieces[source]
    return lax.all_gather(total, axis, axis=0, tiled=True)


def pick_block():
    block_len = 8
    for candidate in range(128, 7, -8):
        block_len = candidate
        break
    return block_len


def pick_group(block_count):
    group_len = 1
    for candidate in range(1, 9):
        if block_count % candidate == 0:
            group_len = candidate
    return group_len


def smoothness(masked_f, weight, send_lists, neighbours, width, gates):
    slots = masked_f.shape[1]
    values = jnp.concatenate([masked_f * weight[None, :], weight[None, :]], axis=0)
    lanes = values.shape[0]
    high = lax.reduce_precision(values, exponent_bits=8, mantissa_bits=7)
    rest = values - high
    middle = lax.reduce_precision(rest, exponent_bits=8, mantissa_bits=7)
    low = rest - middle
    split = jnp.concatenate([high, middle, low], axis=0).astype(jnp.bfloat16)
    rim_index, _ = lax.optimization_barrier((send_lists[0], gates[0]))
    chosen = jnp.arange(slots, dtype=jnp.int32)[:, None] == rim_index.reshape(1, -1)
    chosen_parts = jnp.dot(split, chosen.astype(jnp.bfloat16), preferred_element_type=jnp.float32)
    picked = chosen_parts[:lanes] + chosen_parts[lanes : 2 * lanes] + chosen_parts[2 * lanes :]
    rim = picked.shape[1] // 2
    padded = padded_2(picked, (("cell", 1),), rim)
    rim_vals = jnp.concatenate([padded[:, :rim], padded[:, 3 * rim :]], axis=1)
    rim_high = lax.reduce_precision(rim_vals, exponent_bits=8, mantissa_bits=7)
    rim_rest = rim_vals - rim_high
    rim_middle = lax.reduce_precision(rim_rest, exponent_bits=8, mantissa_bits=7)
    rim_split = jnp.concatenate([rim_high, rim_middle, rim_rest - rim_middle], axis=0)
    rim_split = rim_split.astype(jnp.bfloat16)
    block_len = pick_block()
    block_count = width // block_len
    pieces = 1 + (128 + block_len - 1) // block_len
    spread = jnp.pad(split, ((0, 0), (64, pieces * block_len)))
    local_vals = lax.slice_in_dim(spread, 0, (block_count + pieces - 1) * block_len, axis=1)
    shifted = [
        local_vals[:, m * block_len : (m + block_count) * block_len].reshape(
            3 * lanes, block_count, block_len
        )
        for m in range(pieces)
    ]
    rim_part = jnp.broadcast_to(rim_split[:, None, :], (3 * lanes, block_count, 2 * rim))
    windows = jnp.concatenate(shifted + [rim_part], axis=2).transpose(1, 0, 2)
    span = windows.shape[2]
    position = jnp.arange(width, dtype=jnp.int32)
    anchor = position // block_len * block_len
    column = jnp.where(
        neighbours < slots,
        neighbours - anchor[None, :] + 64,
        jnp.where(neighbours < slots + 2 * rim, pieces * block_len + neighbours - slots, -1),
    )
    column = column.reshape(neighbours.shape[0], block_count, block_len).transpose(1, 0, 2)
    group_len = pick_group(block_count)
    group_count = block_count // group_len
    sums = []
    for g in range(group_count):
        window_set = windows[g * group_len : (g + 1) * group_len]
        column_set = column[g * group_len : (g + 1) * group_len]
        gate = gates[min(g, len(gates) - 1)]
        target = jnp.arange(span, dtype=jnp.int32)[None, None, :, None]
        with jax.named_scope("late_counts" if g >= len(gates) - 1 else f"counts_{g}"):
            column_set, _ = lax.optimization_barrier((column_set, gate))
            hits = jnp.sum((column_set[:, :, None, :] == target).astype(jnp.float32), axis=1)
            hits = hits.astype(jnp.bfloat16)
            part = jnp.einsum(
                "grw,gwb->grb", window_set, hits, preferred_element_type=jnp.float32
            )
        sums.append(part[:, :lanes] + part[:, lanes : 2 * lanes] + part[:, 2 * lanes :])
    sums = jnp.concatenate(sums, axis=0)
    sums = sums.transpose(1, 0, 2).reshape(lanes, width)
    coupling = masked_f * sums[-1][None, :] - sums[:-1]
    return weight[None] * weight[None] * masked_f + weight[None] * coupling


def split_three(values):
    high = lax.reduce_precision(values, exponent_bits=8, mantissa_bits=7)
    rest = values - high
    middle = lax.reduce_precision(rest, exponent_bits=8, mantissa_bits=7)
    low = rest - middle
    return jnp.concatenate([high, middle, low], axis=0).astype(jnp.bfloat16)


def rim_values(values, split, send_lists):
    slots = values.shape[1]
    lanes = values.shape[0]
    index = send_lists[0].reshape(1, -1)
    chosen = jnp.arange(slots, dtype=jnp.int32)[:, None] == index
    parts = jnp.dot(split, chosen.astype(jnp.bfloat16), preferred_element_type=jnp.float32)
    picked = parts[:lanes] + parts[lanes : 2 * lanes] + parts[2 * lanes :]
    rim = picked.shape[1] // 2
    padded = padded_2(picked, (("cell", 1),), rim)
    return jnp.concatenate([padded[:, :rim], padded[:, 3 * rim :]], axis=1)


def smooth_chunk(masked_f, weight, send_lists, neighbours, first, chunk):
    slots = masked_f.shape[1]
    values = jnp.concatenate([masked_f * weight[None, :], weight[None, :]], axis=0)
    lanes = values.shape[0]
    split = split_three(values)
    rim_split = split_three(rim_values(values, split, send_lists))
    reach = 64
    extended = jnp.pad(split, ((0, 0), (reach, reach)))
    local = lax.dynamic_slice_in_dim(extended, first, chunk + 2 * reach, axis=1)
    window = jnp.concatenate([local, rim_split], axis=1)
    faces = lax.dynamic_slice_in_dim(neighbours, first, chunk, axis=1)
    span_local = chunk + 2 * reach
    column = jnp.where(
        faces < slots,
        faces - first + reach,
        jnp.where(faces < slots + rim_split.shape[1], span_local + faces - slots, -1),
    )
    target = jnp.arange(window.shape[1], dtype=jnp.int32)[:, None]
    hits = jnp.zeros((window.shape[1], chunk), jnp.float32)
    for k in range(column.shape[0]):
        hits = hits + (column[k][None, :] == target).astype(jnp.float32)
    parts = jnp.dot(window, hits.astype(jnp.bfloat16), preferred_element_type=jnp.float32)
    sums = parts[:lanes] + parts[lanes : 2 * lanes] + parts[2 * lanes :]
    own_p = lax.dynamic_slice_in_dim(masked_f, first, chunk, axis=1)
    own_w = lax.dynamic_slice_in_dim(weight, first, chunk, axis=0)
    coupling = own_p * sums[-1][None, :] - sums[:-1]
    return own_w[None] * own_w[None] * own_p + own_w[None] * coupling


def on_device(sensitivity, direction, depth_weight, counts, send_lists, neighbours):
    slots = sensitivity.shape[1]
    nvecs = direction.shape[0]
    live = jnp.arange(slots, dtype=jnp.int32) < counts[0]
    masked = jnp.where(live[None, :], direction, jnp.zeros_like(direction))
    partial_data = lax.dot_general(
        masked, sensitivity, (((1,), (1,)), ((), ())), preferred_element_type=jnp.float32
    )
    summed, _ = butterfly_sum(partial_data, "cell")
    rounded = summed.astype(jnp.bfloat16)
    remainder = (summed - rounded.astype(jnp.float32)).astype(jnp.bfloat16)
    stacked = jnp.concatenate([rounded, remainder], axis=0)
    both = jnp.dot(stacked, sensitivity, preferred_element_type=jnp.float32)
    partial_cells = both[:nvecs] + both[nvecs:]
    count = lax.axis_size("dp")
    chunk = slots // count
    me = lax.axis_index("dp")
    first = me * chunk
    pieces = partial_cells.reshape(nvecs, count, chunk).transpose(1, 0, 2)
    pieces = lax.all_to_all(pieces, "dp", 0, 0)
    misfit = pieces[0]
    for source in range(1, count):
        misfit = misfit + pieces[source]
    weight = jnp.where(live, depth_weight, jnp.float32(0.0))
    masked_f = masked.astype(jnp.float32)
    smooth = smooth_chunk(masked_f, weight, send_lists, neighbours, first, chunk)
    total = misfit + 0.5 * smooth
    live_chunk = lax.dynamic_slice_in_dim(live, first, chunk, axis=0)
    product = jnp.where(live_chunk[None, :], total, jnp.float32(0.0))
    return lax.all_gather(product, "dp", axis=1, tiled=True)


def solution(mesh):
    placed = (
        P("dp", "cell"),
        P(None, "cell"),
        P("cell"),
        P("cell"),
        P("cell", None, None),
        P(None, "cell"),
    )
    step = jax.shard_map(
        on_device, mesh=mesh, in_specs=placed, out_specs=P(None, "cell"), check_vma=False
    )
    return step
```

```python
import jax
import jax.numpy as jnp
from jax import lax
from jax.sharding import Mesh, PartitionSpec as P


def padded_2(value, sides, width):
    for axis, dim in sides:
        count, length = (lax.axis_size(axis), value.shape[dim])
        up = [(i, (i + 1) % count) for i in range(count - 1)]
        down = [(j, i) for i, j in up]
        last = lax.slice_in_dim(value, length - width, length, axis=dim)
        leading = lax.slice_in_dim(value, 0, width, axis=dim)
        before = lax.ppermute(last, axis, up)
        after = lax.ppermute(leading, axis, down)
        value = jnp.concatenate([before, value, after], axis=dim)
    return value


def butterfly_sum(value, axis):
    count = lax.axis_size(axis)
    rounds = []
    step = 1
    while step < count:
        pairs = [(j, j ^ step) for j in range(count)]
        value = value + lax.ppermute(value, axis, pairs)
        rounds.append(value)
        step *= 2
    return value, rounds


def halving_sum(value, axis):
    count = lax.axis_size(axis)
    me = lax.axis_index(axis)
    steps = []
    step = 1
    while step < count:
        steps.append(step)
        step *= 2
    for step in steps:
        half = value.shape[0] // 2
        low, high = value[:half], value[half:]
        upper = (me & step) != 0
        keep = jnp.where(upper, high, low)
        send = jnp.where(upper, low, high)
        pairs = [(j, j ^ step) for j in range(count)]
        value = keep + lax.ppermute(send, axis, pairs)
    for step in reversed(steps):
        pairs = [(j, j ^ step) for j in range(count)]
        other = lax.ppermute(value, axis, pairs)
        upper = (me & step) != 0
        low = jnp.where(upper, other, value)
        high = jnp.where(upper, value, other)
        value = jnp.concatenate([low, high], axis=0)
    return value


def exchange_sum(value, axis):
    count = lax.axis_size(axis)
    rows = value.shape[0] // count
    pieces = value.reshape(count, rows, value.shape[1])
    pieces = lax.all_to_all(pieces, axis, 0, 0)
    total = pieces[0]
    for source in range(1, count):
        total = total + pieces[source]
    return lax.all_gather(total, axis, axis=0, tiled=True)


def pick_block():
    block_len = 8
    for candidate in range(128, 7, -8):
        block_len = candidate
        break
    return block_len


def pick_group(block_count):
    group_len = 1
    for candidate in range(1, 9):
        if block_count % candidate == 0:
            group_len = candidate
    return group_len


def smoothness(masked_f, weight, send_lists, neighbours, width, gates):
    slots = masked_f.shape[1]
    values = jnp.concatenate([masked_f * weight[None, :], weight[None, :]], axis=0)
    lanes = values.shape[0]
    high = lax.reduce_precision(values, exponent_bits=8, mantissa_bits=7)
    rest = values - high
    middle = lax.reduce_precision(rest, exponent_bits=8, mantissa_bits=7)
    low = rest - middle
    split = jnp.concatenate([high, middle, low], axis=0).astype(jnp.bfloat16)
    rim_index, _ = lax.optimization_barrier((send_lists[0], gates[0]))
    chosen = jnp.arange(slots, dtype=jnp.int32)[:, None] == rim_index.reshape(1, -1)
    chosen_parts = jnp.dot(split, chosen.astype(jnp.bfloat16), preferred_element_type=jnp.float32)
    picked = chosen_parts[:lanes] + chosen_parts[lanes : 2 * lanes] + chosen_parts[2 * lanes :]
    rim = picked.shape[1] // 2
    padded = padded_2(picked, ((CELL, 1),), rim)
    rim_vals = jnp.concatenate([padded[:, :rim], padded[:, 3 * rim :]], axis=1)
    rim_high = lax.reduce_precision(rim_vals, exponent_bits=8, mantissa_bits=7)
    rim_rest = rim_vals - rim_high
    rim_middle = lax.reduce_precision(rim_rest, exponent_bits=8, mantissa_bits=7)
    rim_split = jnp.concatenate([rim_high, rim_middle, rim_rest - rim_middle], axis=0)
    rim_split = rim_split.astype(jnp.bfloat16)
    block_len = pick_block()
    block_count = width // block_len
    pieces = 1 + (128 + block_len - 1) // block_len
    spread = jnp.pad(split, ((0, 0), (64, pieces * block_len)))
    local_vals = lax.slice_in_dim(spread, 0, (block_count + pieces - 1) * block_len, axis=1)
    shifted = [
        local_vals[:, m * block_len : (m + block_count) * block_len].reshape(
            3 * lanes, block_count, block_len
        )
        for m in range(pieces)
    ]
    rim_part = jnp.broadcast_to(rim_split[:, None, :], (3 * lanes, block_count, 2 * rim))
    windows = jnp.concatenate(shifted + [rim_part], axis=2).transpose(1, 0, 2)
    span = windows.shape[2]
    position = jnp.arange(width, dtype=jnp.int32)
    anchor = position // block_len * block_len
    column = jnp.where(
        neighbours < slots,
        neighbours - anchor[None, :] + 64,
        jnp.where(neighbours < slots + 2 * rim, pieces * block_len + neighbours - slots, -1),
    )
    column = column.reshape(neighbours.shape[0], block_count, block_len).transpose(1, 0, 2)
    group_len = pick_group(block_count)
    group_count = block_count // group_len
    sums = []
    for g in range(group_count):
        window_set = windows[g * group_len : (g + 1) * group_len]
        column_set = column[g * group_len : (g + 1) * group_len]
        gate = gates[min(g, len(gates) - 1)]
        target = jnp.arange(span, dtype=jnp.int32)[None, None, :, None]
        with jax.named_scope("late_counts" if g >= len(gates) - 1 else f"counts_{g}"):
            column_set, _ = lax.optimization_barrier((column_set, gate))
            hits = jnp.sum((column_set[:, :, None, :] == target).astype(jnp.float32), axis=1)
            hits = hits.astype(jnp.bfloat16)
            part = jnp.einsum(
                "grw,gwb->grb", window_set, hits, preferred_element_type=jnp.float32
            )
        sums.append(part[:, :lanes] + part[:, lanes : 2 * lanes] + part[:, 2 * lanes :])
    sums = jnp.concatenate(sums, axis=0)
    sums = sums.transpose(1, 0, 2).reshape(lanes, width)
    coupling = masked_f * sums[-1][None, :] - sums[:-1]
    return weight[None] * weight[None] * masked_f + weight[None] * coupling


def split_three(values):
    high = lax.reduce_precision(values, exponent_bits=8, mantissa_bits=7)
    rest = values - high
    middle = lax.reduce_precision(rest, exponent_bits=8, mantissa_bits=7)
    low = rest - middle
    return jnp.concatenate([high, middle, low], axis=0).astype(jnp.bfloat16)


def rim_values(values, split, send_lists):
    slots = values.shape[1]
    lanes = values.shape[0]
    index = send_lists[0].reshape(1, -1)
    chosen = jnp.arange(slots, dtype=jnp.int32)[:, None] == index
    parts = jnp.dot(split, chosen.astype(jnp.bfloat16), preferred_element_type=jnp.float32)
    picked = parts[:lanes] + parts[lanes : 2 * lanes] + parts[2 * lanes :]
    rim = picked.shape[1] // 2
    padded = padded_2(picked, ((CELL, 1),), rim)
    return jnp.concatenate([padded[:, :rim], padded[:, 3 * rim :]], axis=1)


def smooth_chunk(masked_f, weight, send_lists, neighbours, first, chunk):
    slots = masked_f.shape[1]
    values = jnp.concatenate([masked_f * weight[None, :], weight[None, :]], axis=0)
    lanes = values.shape[0]
    split = split_three(values)
    rim_split = split_three(rim_values(values, split, send_lists))
    reach = 64
    extended = jnp.pad(split, ((0, 0), (reach, reach)))
    local = lax.dynamic_slice_in_dim(extended, first, chunk + 2 * reach, axis=1)
    window = jnp.concatenate([local, rim_split], axis=1)
    faces = lax.dynamic_slice_in_dim(neighbours, first, chunk, axis=1)
    span_local = chunk + 2 * reach
    column = jnp.where(
        faces < slots,
        faces - first + reach,
        jnp.where(faces < slots + rim_split.shape[1], span_local + faces - slots, -1),
    )
    target = jnp.arange(window.shape[1], dtype=jnp.int32)[:, None]
    hits = jnp.zeros((window.shape[1], chunk), jnp.float32)
    for k in range(column.shape[0]):
        hits = hits + (column[k][None, :] == target).astype(jnp.float32)
    parts = jnp.dot(window, hits.astype(jnp.bfloat16), preferred_element_type=jnp.float32)
    sums = parts[:lanes] + parts[lanes : 2 * lanes] + parts[2 * lanes :]
    own_p = lax.dynamic_slice_in_dim(masked_f, first, chunk, axis=1)
    own_w = lax.dynamic_slice_in_dim(weight, first, chunk, axis=0)
    coupling = own_p * sums[-1][None, :] - sums[:-1]
    return own_w[None] * own_w[None] * own_p + own_w[None] * coupling


def on_device(sensitivity, direction, depth_weight, counts, send_lists, neighbours):
    slots = sensitivity.shape[1]
    nvecs = direction.shape[0]
    live = jnp.arange(slots, dtype=jnp.int32) < counts[0]
    masked = jnp.where(live[None, :], direction, jnp.zeros_like(direction))
    partial_data = lax.dot_general(
        masked, sensitivity, (((1,), (1,)), ((), ())), preferred_element_type=jnp.float32
    )
    summed = lax.psum(lax.psum(partial_data, "z"), "x")
    rounded = summed.astype(jnp.bfloat16)
    remainder = (summed - rounded.astype(jnp.float32)).astype(jnp.bfloat16)
    stacked = jnp.concatenate([rounded, remainder], axis=0)
    both = jnp.dot(stacked, sensitivity, preferred_element_type=jnp.float32)
    partial_cells = both[:nvecs] + both[nvecs:]
    count = lax.axis_size(DP)
    chunk = slots // count
    me = lax.axis_index(DP)
    first = me * chunk
    pieces = partial_cells.reshape(nvecs, count, chunk).transpose(1, 0, 2)
    pieces = lax.all_to_all(pieces, DP, 0, 0)
    misfit = pieces[0]
    for source in range(1, count):
        misfit = misfit + pieces[source]
    weight = jnp.where(live, depth_weight, jnp.float32(0.0))
    masked_f = masked.astype(jnp.float32)
    smooth = smooth_chunk(masked_f, weight, send_lists, neighbours, first, chunk)
    total = misfit + 0.5 * smooth
    live_chunk = lax.dynamic_slice_in_dim(live, first, chunk, axis=0)
    product = jnp.where(live_chunk[None, :], total, jnp.float32(0.0))
    return lax.all_gather(product, DP, axis=1, tiled=True)


DP = ("y", "core")
CELL = ("x", "z")


def solution(mesh):
    dp_size, cell_size = mesh.devices.shape
    z_size = 8 if cell_size % 8 == 0 else cell_size
    split_mesh = Mesh(
        mesh.devices.reshape(dp_size // 2, 2, cell_size // z_size, z_size), DP + CELL
    )
    placed = (
        P(DP, CELL),
        P(None, CELL),
        P(CELL),
        P(CELL),
        P(CELL, None, None),
        P(None, CELL),
    )
    step = jax.shard_map(
        on_device, mesh=split_mesh, in_specs=placed, out_specs=P(None, CELL), check_vma=False
    )
    return step
```

```python
import jax
import jax.numpy as jnp
from jax import lax
from jax.sharding import Mesh, PartitionSpec as P


def padded_2(value, sides, width):
    for axis, dim in sides:
        count, length = (lax.axis_size(axis), value.shape[dim])
        up = [(i, (i + 1) % count) for i in range(count - 1)]
        down = [(j, i) for i, j in up]
        last = lax.slice_in_dim(value, length - width, length, axis=dim)
        leading = lax.slice_in_dim(value, 0, width, axis=dim)
        before = lax.ppermute(last, axis, up)
        after = lax.ppermute(leading, axis, down)
        value = jnp.concatenate([before, value, after], axis=dim)
    return value


def split_three(values):
    high = lax.reduce_precision(values, exponent_bits=8, mantissa_bits=7)
    rest = values - high
    middle = lax.reduce_precision(rest, exponent_bits=8, mantissa_bits=7)
    low = rest - middle
    return jnp.concatenate([high, middle, low], axis=0).astype(jnp.bfloat16)


def rim_values(values, split, send_lists):
    slots = values.shape[1]
    lanes = values.shape[0]
    index = send_lists[0].reshape(1, -1)
    chosen = jnp.arange(slots, dtype=jnp.int32)[:, None] == index
    parts = jnp.dot(split, chosen.astype(jnp.bfloat16), preferred_element_type=jnp.float32)
    picked = parts[:lanes] + parts[lanes : 2 * lanes] + parts[2 * lanes :]
    rim = picked.shape[1] // 2
    padded = padded_2(picked, ((CELL, 1),), rim)
    return jnp.concatenate([padded[:, :rim], padded[:, 3 * rim :]], axis=1)


def smooth_chunk(masked_f, weight, send_lists, neighbours, first, chunk):
    slots = masked_f.shape[1]
    values = jnp.concatenate([masked_f * weight[None, :], weight[None, :]], axis=0)
    lanes = values.shape[0]
    split = split_three(values)
    rim_split = split_three(rim_values(values, split, send_lists))
    reach = 64
    extended = jnp.pad(split, ((0, 0), (reach, reach)))
    local = lax.dynamic_slice_in_dim(extended, first, chunk + 2 * reach, axis=1)
    window = jnp.concatenate([local, rim_split], axis=1)
    faces = lax.dynamic_slice_in_dim(neighbours, first, chunk, axis=1)
    span_local = chunk + 2 * reach
    column = jnp.where(
        faces < slots,
        faces - first + reach,
        jnp.where(faces < slots + rim_split.shape[1], span_local + faces - slots, -1),
    )
    target = jnp.arange(window.shape[1], dtype=jnp.int32)[:, None]
    hits = jnp.zeros((window.shape[1], chunk), jnp.float32)
    for k in range(column.shape[0]):
        hits = hits + (column[k][None, :] == target).astype(jnp.float32)
    parts = jnp.dot(window, hits.astype(jnp.bfloat16), preferred_element_type=jnp.float32)
    sums = parts[:lanes] + parts[lanes : 2 * lanes] + parts[2 * lanes :]
    own_p = lax.dynamic_slice_in_dim(masked_f, first, chunk, axis=1)
    own_w = lax.dynamic_slice_in_dim(weight, first, chunk, axis=0)
    coupling = own_p * sums[-1][None, :] - sums[:-1]
    return own_w[None] * own_w[None] * own_p + own_w[None] * coupling


def on_device_body(sensitivity, direction, depth_weight, counts, send_lists, neighbours):
    slots = sensitivity.shape[1]
    nvecs = direction.shape[0]
    live = jnp.arange(slots, dtype=jnp.int32) < counts[0]
    masked = jnp.where(live[None, :], direction, jnp.zeros_like(direction))
    partial_data = lax.dot_general(
        masked, sensitivity, (((1,), (1,)), ((), ())), preferred_element_type=jnp.float32
    )
    summed = lax.psum(lax.psum(partial_data, "z"), "x")
    rounded = summed.astype(jnp.bfloat16)
    remainder = (summed - rounded.astype(jnp.float32)).astype(jnp.bfloat16)
    stacked = jnp.concatenate([rounded, remainder], axis=0)
    both = jnp.dot(stacked, sensitivity, preferred_element_type=jnp.float32)
    partial_cells = both[:nvecs] + both[nvecs:]
    count = lax.axis_size(DP)
    chunk = slots // count
    me = lax.axis_index(DP)
    first = me * chunk
    pieces = partial_cells.reshape(nvecs, count, chunk).transpose(1, 0, 2)
    pieces = lax.all_to_all(pieces, DP, 0, 0)
    misfit = pieces[0]
    for source in range(1, count):
        misfit = misfit + pieces[source]
    weight = jnp.where(live, depth_weight, jnp.float32(0.0))
    masked_f = masked.astype(jnp.float32)
    smooth = smooth_chunk(masked_f, weight, send_lists, neighbours, first, chunk)
    total = misfit + 0.5 * smooth
    live_chunk = lax.dynamic_slice_in_dim(live, first, chunk, axis=0)
    product = jnp.where(live_chunk[None, :], total, jnp.float32(0.0))
    gathered = lax.all_gather(product, DP, axis=0)
    return gathered.transpose(1, 0, 2).reshape(nvecs, slots)


DP = ("y", "core")
CELL = ("x", "z")


def solution(mesh):
    dp_size, cell_size = mesh.devices.shape
    z_size = 8 if cell_size % 8 == 0 else cell_size
    split_mesh = Mesh(
        mesh.devices.reshape(dp_size // 2, 2, cell_size // z_size, z_size), DP + CELL
    )
    placed = (
        P(DP, CELL),
        P(None, CELL),
        P(CELL),
        P(CELL),
        P(CELL, None, None),
        P(None, CELL),
    )
    return jax.shard_map(
        on_device_body, mesh=split_mesh, in_specs=placed, out_specs=P(None, CELL), check_vma=False
    )
```

```python
import jax
import jax.numpy as jnp
from jax import lax
from jax.sharding import Mesh, PartitionSpec as P


def padded_2(value, sides, width):
    for axis, dim in sides:
        count, length = (lax.axis_size(axis), value.shape[dim])
        up = [(i, (i + 1) % count) for i in range(count - 1)]
        down = [(j, i) for i, j in up]
        last = lax.slice_in_dim(value, length - width, length, axis=dim)
        leading = lax.slice_in_dim(value, 0, width, axis=dim)
        before = lax.ppermute(last, axis, up)
        after = lax.ppermute(leading, axis, down)
        value = jnp.concatenate([before, value, after], axis=dim)
    return value


def split_three(values):
    high = lax.reduce_precision(values, exponent_bits=8, mantissa_bits=7)
    rest = values - high
    middle = lax.reduce_precision(rest, exponent_bits=8, mantissa_bits=7)
    low = rest - middle
    return jnp.concatenate([high, middle, low], axis=0).astype(jnp.bfloat16)


def rim_values(values, split, send_lists):
    slots = values.shape[1]
    lanes = values.shape[0]
    index = send_lists[0].reshape(1, -1)
    chosen = jnp.arange(slots, dtype=jnp.int32)[:, None] == index
    parts = jnp.dot(split, chosen.astype(jnp.bfloat16), preferred_element_type=jnp.float32)
    picked = parts[:lanes] + parts[lanes : 2 * lanes] + parts[2 * lanes :]
    rim = picked.shape[1] // 2
    padded = padded_2(picked, ((CELL, 1),), rim)
    return jnp.concatenate([padded[:, :rim], padded[:, 3 * rim :]], axis=1)


def smooth_chunk(masked_f, weight, send_lists, neighbours, first, chunk):
    slots = masked_f.shape[1]
    values = jnp.concatenate([masked_f * weight[None, :], weight[None, :]], axis=0)
    lanes = values.shape[0]
    split = split_three(values)
    rim_split = split_three(rim_values(values, split, send_lists))
    reach = 64
    extended = jnp.pad(split, ((0, 0), (reach, reach)))
    local = lax.dynamic_slice_in_dim(extended, first, chunk + 2 * reach, axis=1)
    window = jnp.concatenate([local, rim_split], axis=1)
    faces = lax.dynamic_slice_in_dim(neighbours, first, chunk, axis=1)
    span_local = chunk + 2 * reach
    column = jnp.where(
        faces < slots,
        faces - first + reach,
        jnp.where(faces < slots + rim_split.shape[1], span_local + faces - slots, -1),
    )
    target = jnp.arange(window.shape[1], dtype=jnp.int32)[:, None]
    hits = jnp.zeros((window.shape[1], chunk), jnp.float32)
    for k in range(column.shape[0]):
        hits = hits + (column[k][None, :] == target).astype(jnp.float32)
    parts = jnp.dot(window, hits.astype(jnp.bfloat16), preferred_element_type=jnp.float32)
    sums = parts[:lanes] + parts[lanes : 2 * lanes] + parts[2 * lanes :]
    own_p = lax.dynamic_slice_in_dim(masked_f, first, chunk, axis=1)
    own_w = lax.dynamic_slice_in_dim(weight, first, chunk, axis=0)
    coupling = own_p * sums[-1][None, :] - sums[:-1]
    return own_w[None] * own_w[None] * own_p + own_w[None] * coupling


def on_device_body(sensitivity, direction, depth_weight, counts, send_lists, neighbours):
    slots = sensitivity.shape[1]
    nvecs = direction.shape[0]
    live = jnp.arange(slots, dtype=jnp.int32) < counts[0]
    masked = jnp.where(live[None, :], direction, jnp.zeros_like(direction))
    partial_data = lax.dot_general(
        masked, sensitivity, (((1,), (1,)), ((), ())), preferred_element_type=jnp.float32
    )
    summed = lax.psum(lax.psum(partial_data, "z"), "x")
    rounded = summed.astype(jnp.bfloat16)
    remainder = (summed - rounded.astype(jnp.float32)).astype(jnp.bfloat16)
    stacked = jnp.concatenate([rounded, remainder], axis=0)
    both = jnp.dot(stacked, sensitivity, preferred_element_type=jnp.float32)
    partial_cells = both[:nvecs] + both[nvecs:]
    count = lax.axis_size(DP)
    chunk = slots // count
    me = lax.axis_index(DP)
    first = me * chunk
    pieces = partial_cells.reshape(nvecs, count, chunk)
    pieces = lax.all_to_all(pieces, DP, 1, 1)
    misfit = pieces[:, 0]
    for source in range(1, count):
        misfit = misfit + pieces[:, source]
    weight = jnp.where(live, depth_weight, jnp.float32(0.0))
    masked_f = masked.astype(jnp.float32)
    smooth = smooth_chunk(masked_f, weight, send_lists, neighbours, first, chunk)
    total = misfit + 0.5 * smooth
    live_chunk = lax.dynamic_slice_in_dim(live, first, chunk, axis=0)
    product = jnp.where(live_chunk[None, :], total, jnp.float32(0.0))
    return lax.all_gather(product, DP, axis=1, tiled=True)


DP = ("y", "core")
CELL = ("x", "z")


def solution(mesh):
    dp_size, cell_size = mesh.devices.shape
    z_size = 8 if cell_size % 8 == 0 else cell_size
    split_mesh = Mesh(
        mesh.devices.reshape(dp_size // 2, 2, cell_size // z_size, z_size), DP + CELL
    )
    placed = (
        P(DP, CELL),
        P(None, CELL),
        P(CELL),
        P(CELL),
        P(CELL, None, None),
        P(None, CELL),
    )
    return jax.shard_map(
        on_device_body, mesh=split_mesh, in_specs=placed, out_specs=P(None, CELL), check_vma=False
    )
```
